32 devices in a mesh: shard: 4 (over z), rep: 8 (over y, x, core).
Axes of the slice: x: 2, y: 2, z: 4, core: 2. Of those that a mesh axis runs over, the one named last changes fastest.
Arguments:
- grads: bfloat16 [1, 8192, 28672], P(None, 'shard', 'rep'), may hold values from -81 to 81
- seeds: int32 [1], replicated, may hold values from 0 to 999999
Outputs:
- projected: bfloat16 [512, 1, 28672], P('shard', None, 'rep')
The draws below stay inside these ranges and needn't reach their ends.
All inputs are finite; a program needn't handle non-finite values.
Results may differ from the reference program's by a relative error of at most 0.0056.
Values may be sent and summed in bfloat16 or wider, within the bound.
No kernel may reach another device: no remote copies, remote signals or barrier semaphores. Data moves between devices by JAX's collectives and lax.ppermute only.
A program may use at most 128 MiB of HBM per device.

```python
import math
import jax
import jax.numpy as jnp
from jax import lax

D = 8192
FF = 28672
RANK = 512
MATS = 1


def draw_grads(key, part):
    key_noise, key_rows, key_cols = jax.random.split(key, 3)
    row_place = (jnp.arange(D, dtype=jnp.float32) / D)[None, :, None]
    col_place = (jnp.arange(FF, dtype=jnp.float32) / FF)[None, None, :]
    row_scale = 0.1 * jnp.exp(math.log(3.0) * row_place + math.log(10.0) * jax.random.uniform(key_rows, (MATS, D, 1), jnp.float32))
    col_scale = 0.1 * jnp.exp(math.log(3.0) * col_place + math.log(10.0) * jax.random.uniform(key_cols, (MATS, 1, FF), jnp.float32))
    noise = jnp.clip(jax.random.normal(key_noise, (MATS, D, FF), jnp.float32), -6.0, 6.0)
    return (noise * row_scale * col_scale).astype(jnp.bfloat16)


def setup_inputs(seed: int = 0) -> dict:
    arg_keys = jax.random.split(jax.random.key(seed), 3)
    return {
        "grads": draw_grads(jax.random.fold_in(arg_keys[2], 71), 0),
        "seeds": jax.random.randint(arg_keys[1], (MATS,), 0, 1000000).astype(jnp.int32),
    }


mix_first = 668265263
mix_second = -2048144789
mix_third = -1028477387

def sketch_table(seeds, first_row, count, rank):
    rows = first_row + jnp.arange(count, dtype=jnp.int32)
    columns = jnp.arange(rank, dtype=jnp.int32)
    counter = rows[:, None] * jnp.int32(rank) + columns[None, :]
    hashed = jnp.bitwise_xor(counter[None, :, :], (seeds * jnp.int32(mix_first))[:, None, None])
    hashed = hashed * jnp.int32(mix_second)
    hashed = jnp.bitwise_xor(hashed, lax.shift_right_logical(hashed, jnp.int32(15)))
    hashed = hashed * jnp.int32(mix_third)
    hashed = jnp.bitwise_xor(hashed, lax.shift_right_logical(hashed, jnp.int32(13)))
    unit = lax.shift_right_logical(hashed, jnp.int32(8)).astype(jnp.float32) * (1.0 / 16777216.0)
    return (2.0 * unit - 1.0).astype(jnp.bfloat16)

def reference(grads, seeds):
    results = []
    for matrix in range(MATS):
        omega = sketch_table(seeds[matrix:matrix + 1], jnp.int32(0), FF, RANK)[0]
        sketch = jnp.dot(grads[matrix].astype(jnp.float32), omega.astype(jnp.float32), preferred_element_type=jnp.float32)
        gram = jnp.dot(sketch.T.astype(jnp.float32), sketch.astype(jnp.float32), precision=lax.Precision.HIGHEST, preferred_element_type=jnp.float32)
        factor = jnp.linalg.cholesky(gram)
        basis = lax.linalg.triangular_solve(factor, sketch, left_side=False, lower=True, transpose_a=True)
        basis = basis.astype(jnp.bfloat16)
        projected = jnp.dot(basis.T.astype(jnp.float32), grads[matrix].astype(jnp.float32), preferred_element_type=jnp.float32)
        results.append(projected.astype(jnp.bfloat16))
    return jnp.stack(results, axis=1)
```

```python
import jax
import jax.numpy as jnp
from jax import lax
from jax.sharding import PartitionSpec as P

RANK = 512


mix_first = 668265263
mix_second = -2048144789
mix_third = -1028477387


def sketch_table(seeds, first_row, count, rank):
    rows = first_row + lax.iota(jnp.int32, count)
    columns = lax.iota(jnp.int32, rank)
    counter = rows[:, None] * jnp.int32(rank) + columns[None, :]
    hashed = jnp.bitwise_xor(counter[None, :, :], (seeds * jnp.int32(mix_first))[:, None, None])
    hashed = hashed * jnp.int32(mix_second)
    hashed = jnp.bitwise_xor(hashed, lax.shift_right_logical(hashed, jnp.int32(15)))
    hashed = hashed * jnp.int32(mix_third)
    hashed = jnp.bitwise_xor(hashed, lax.shift_right_logical(hashed, jnp.int32(13)))
    unit = lax.shift_right_logical(hashed, jnp.int32(8)).astype(jnp.float32) * (1.0 / 16777216.0)
    return (2.0 * unit - 1.0).astype(jnp.bfloat16)


def body(grads, seeds):
    mats, depth, width = grads.shape
    col0 = lax.axis_index("rep") * width
    outs = []
    for m in range(mats):
        table = sketch_table(seeds[m:m + 1], col0, width, RANK)[0]
        g = grads[m]
        partial = jnp.dot(g, table, preferred_element_type=jnp.float32)
        sketch_rows = lax.psum(partial, "rep")
        local_gram = jnp.dot(
            sketch_rows.T, sketch_rows,
            precision=lax.Precision.HIGHEST,
            preferred_element_type=jnp.float32,
        )
        gram = lax.psum(local_gram, "shard")
        factor = jnp.linalg.cholesky(gram)
        basis_rows = lax.linalg.triangular_solve(
            factor, sketch_rows, left_side=False, lower=True, transpose_a=True
        ).astype(jnp.bfloat16)
        partial_sum = jnp.dot(basis_rows.T, g, preferred_element_type=jnp.float32)
        outs.append(partial_sum)
    partial_sum = jnp.stack(outs, axis=1)
    projected = lax.psum_scatter(partial_sum, "shard", scatter_dimension=0, tiled=True)
    return projected.astype(jnp.bfloat16)


def solution(mesh):
    return jax.shard_map(
        body,
        mesh=mesh,
        in_specs=(P(None, "shard", "rep"), P()),
        out_specs=P("shard", None, "rep"),
        check_vma=False,
    )
```

```python
import jax
import jax.numpy as jnp
from jax import lax
from jax.sharding import PartitionSpec as P

RANK = 512


mix_first = 668265263
mix_second = -2048144789
mix_third = -1028477387


def sketch_table(seeds, first_row, count, rank):
    rows = first_row + lax.iota(jnp.int32, count)
    columns = lax.iota(jnp.int32, rank)
    counter = rows[:, None] * jnp.int32(rank) + columns[None, :]
    hashed = jnp.bitwise_xor(counter[None, :, :], (seeds * jnp.int32(mix_first))[:, None, None])
    hashed = hashed * jnp.int32(mix_second)
    hashed = jnp.bitwise_xor(hashed, lax.shift_right_logical(hashed, jnp.int32(15)))
    hashed = hashed * jnp.int32(mix_third)
    hashed = jnp.bitwise_xor(hashed, lax.shift_right_logical(hashed, jnp.int32(13)))
    unit = lax.shift_right_logical(hashed, jnp.int32(8)).astype(jnp.float32) * (1.0 / 16777216.0)
    return (2.0 * unit - 1.0).astype(jnp.bfloat16)


def body(grads, seeds):
    mats, depth, width = grads.shape
    col0 = lax.axis_index("rep") * width
    outs = []
    for m in range(mats):
        table = sketch_table(seeds[m:m + 1], col0, width, RANK)[0]
        g = grads[m]
        partial = jnp.dot(g, table, preferred_element_type=jnp.float32)
        sketch_rows = lax.psum(partial, "rep")
        local_gram = jnp.dot(
            sketch_rows.T, sketch_rows,
            precision=lax.Precision.HIGHEST,
            preferred_element_type=jnp.float32,
        )
        piece = local_gram.shape[0] // lax.axis_size("rep")
        mine = lax.dynamic_slice_in_dim(
            local_gram, lax.axis_index("rep") * piece, piece, 0
        )
        gram = lax.all_gather(lax.psum(mine, "shard"), "rep", axis=0, tiled=True)
        factor = jnp.linalg.cholesky(gram)
        basis_rows = lax.linalg.triangular_solve(
            factor, sketch_rows, left_side=False, lower=True, transpose_a=True
        ).astype(jnp.bfloat16)
        partial_sum = jnp.dot(basis_rows.T, g, preferred_element_type=jnp.float32)
        outs.append(partial_sum)
    partial_sum = jnp.stack(outs, axis=1)
    projected = lax.psum_scatter(partial_sum, "shard", scatter_dimension=0, tiled=True)
    return projected.astype(jnp.bfloat16)


def solution(mesh):
    return jax.shard_map(
        body,
        mesh=mesh,
        in_specs=(P(None, "shard", "rep"), P()),
        out_specs=P("shard", None, "rep"),
        check_vma=False,
    )
```

```python
import jax
import jax.numpy as jnp
from jax import lax
from jax.experimental import pallas as pl
from jax.experimental.pallas import tpu as pltpu
from jax.sharding import PartitionSpec as P

RANK = 512
BLOCK = 128


def _mm(a, b, trans_b=False):
    dims = (((1,), (1,)), ((), ())) if trans_b else (((1,), (0,)), ((), ()))
    return lax.dot_general(a, b, dims, precision=lax.Precision.HIGHEST,
                           preferred_element_type=jnp.float32)


def _chol_inv_kernel(g_ref, w_ref, a_ref, d_ref):
    n = g_ref.shape[0]
    b = BLOCK
    a_ref[...] = g_ref[...]
    rows = lax.broadcasted_iota(jnp.int32, (n, n), 0)
    cols = lax.broadcasted_iota(jnp.int32, (n, n), 1)
    w_ref[...] = jnp.where(rows == cols, 1.0, 0.0).astype(jnp.float32)
    lane = lax.broadcasted_iota(jnp.int32, (1, b), 1)
    sub = lax.broadcasted_iota(jnp.int32, (b, 1), 0)
    brow = lax.broadcasted_iota(jnp.int32, (b, b), 0)
    sub8 = lax.broadcasted_iota(jnp.int32, (8, 1), 0)
    bcol = lax.broadcasted_iota(jnp.int32, (b, b), 1)
    for p in range(n // b):
        lo = p * b
        d_ref[...] = jnp.where(brow == bcol, 1.0, 0.0).astype(jnp.float32)

        def step(k, carry):
            base = pl.multiple_of((k // 8) * 8, 8)
            pick = sub8 == (k - base)
            slab = a_ref[pl.ds(lo + base, 8), pl.ds(lo, b)]
            row = jnp.sum(jnp.where(pick, slab, 0.0), axis=0, keepdims=True)
            diag = jnp.sum(jnp.where(lane == k, row, 0.0), axis=1, keepdims=True)
            root = jnp.sqrt(diag)
            lrow = jnp.where(lane >= k, row / root, 0.0)
            lcol = jnp.transpose(jnp.broadcast_to(lrow, (8, b)))[:, 0:1]
            blk = a_ref[lo:lo + b, lo:lo + b]
            a_ref[lo:lo + b, lo:lo + b] = blk - lcol * lrow
            dslab = d_ref[pl.ds(base, 8), :]
            wk = jnp.sum(jnp.where(pick, dslab, 0.0), axis=0, keepdims=True) / root
            strict = jnp.where(sub > k, lcol, 0.0)
            cur = d_ref[...]
            d_ref[...] = jnp.where(brow == k, wk, cur - strict * wk)
            return carry

        lax.fori_loop(0, b, step, 0)
        winv = d_ref[...]
        top = w_ref[lo:lo + b, :]
        newtop = _mm(winv, top)
        w_ref[lo:lo + b, :] = newtop
        hi = lo + b
        if hi < n:
            panel = _mm(a_ref[hi:, lo:lo + b], winv, trans_b=True)
            a_ref[hi:, hi:] = a_ref[hi:, hi:] - _mm(panel, panel, trans_b=True)
            w_ref[hi:, :] = w_ref[hi:, :] - _mm(panel, newtop)


def chol_inverse(gram):
    n = gram.shape[0]
    return pl.pallas_call(
        _chol_inv_kernel,
        out_shape=jax.ShapeDtypeStruct((n, n), jnp.float32),
        in_specs=[pl.BlockSpec(memory_space=pltpu.VMEM)],
        out_specs=pl.BlockSpec(memory_space=pltpu.VMEM),
        scratch_shapes=[pltpu.VMEM((n, n), jnp.float32), pltpu.VMEM((BLOCK, BLOCK), jnp.float32)],
    )(gram)


mix_first = 668265263
mix_second = -2048144789
mix_third = -1028477387


def sketch_table(seeds, first_row, count, rank):
    rows = first_row + lax.iota(jnp.int32, count)
    columns = lax.iota(jnp.int32, rank)
    counter = rows[:, None] * jnp.int32(rank) + columns[None, :]
    hashed = jnp.bitwise_xor(counter[None, :, :], (seeds * jnp.int32(mix_first))[:, None, None])
    hashed = hashed * jnp.int32(mix_second)
    hashed = jnp.bitwise_xor(hashed, lax.shift_right_logical(hashed, jnp.int32(15)))
    hashed = hashed * jnp.int32(mix_third)
    hashed = jnp.bitwise_xor(hashed, lax.shift_right_logical(hashed, jnp.int32(13)))
    unit = lax.shift_right_logical(hashed, jnp.int32(8)).astype(jnp.float32) * (1.0 / 16777216.0)
    return (2.0 * unit - 1.0).astype(jnp.bfloat16)


def body(grads, seeds):
    mats, depth, width = grads.shape
    col0 = lax.axis_index("rep") * width
    outs = []
    for m in range(mats):
        table = sketch_table(seeds[m:m + 1], col0, width, RANK)[0]
        g = grads[m]
        partial = jnp.dot(g, table, preferred_element_type=jnp.float32)
        sketch_rows = lax.psum(partial, "rep")
        local_gram = jnp.dot(
            sketch_rows.T, sketch_rows,
            precision=lax.Precision.HIGHEST,
            preferred_element_type=jnp.float32,
        )
        gram = lax.psum(local_gram, "shard")
        inverse = chol_inverse(gram)
        basis_rows = _mm(sketch_rows, inverse, trans_b=True).astype(jnp.bfloat16)
        partial_sum = jnp.dot(basis_rows.T, g, preferred_element_type=jnp.float32)
        outs.append(partial_sum)
    partial_sum = jnp.stack(outs, axis=1)
    projected = lax.psum_scatter(partial_sum, "shard", scatter_dimension=0, tiled=True)
    return projected.astype(jnp.bfloat16)


def solution(mesh):
    return jax.shard_map(
        body,
        mesh=mesh,
        in_specs=(P(None, "shard", "rep"), P()),
        out_specs=P("shard", None, "rep"),
        check_vma=False,
    )
```

```python
import jax
import jax.numpy as jnp
from jax import lax
from jax.sharding import PartitionSpec as P

RANK = 512


mix_first = 668265263
mix_second = -2048144789
mix_third = -1028477387


def sketch_table(seeds, first_row, count, rank):
    rows = first_row + lax.iota(jnp.int32, count)
    columns = lax.iota(jnp.int32, rank)
    counter = rows[:, None] * jnp.int32(rank) + columns[None, :]
    hashed = jnp.bitwise_xor(counter[None, :, :], (seeds * jnp.int32(mix_first))[:, None, None])
    hashed = hashed * jnp.int32(mix_second)
    hashed = jnp.bitwise_xor(hashed, lax.shift_right_logical(hashed, jnp.int32(15)))
    hashed = hashed * jnp.int32(mix_third)
    hashed = jnp.bitwise_xor(hashed, lax.shift_right_logical(hashed, jnp.int32(13)))
    unit = lax.shift_right_logical(hashed, jnp.int32(8)).astype(jnp.float32) * (1.0 / 16777216.0)
    return (2.0 * unit - 1.0).astype(jnp.bfloat16)


def body(grads, seeds):
    mats, depth, width = grads.shape
    col0 = lax.axis_index("rep") * width
    outs = []
    for m in range(mats):
        table = sketch_table(seeds[m:m + 1], col0, width, RANK)[0]
        g = grads[m]
        partial = jnp.dot(g, table, preferred_element_type=jnp.float32)
        sketch_rows = lax.psum(partial, "rep")
        local_gram = jnp.dot(
            sketch_rows.T, sketch_rows,
            precision=lax.Precision.HIGHEST,
            preferred_element_type=jnp.float32,
        )
        gram = lax.psum(local_gram, "shard")
        factor = jnp.linalg.cholesky(gram)
        basis_rows = lax.linalg.triangular_solve(
            factor, sketch_rows, left_side=False, lower=True, transpose_a=True
        ).astype(jnp.bfloat16)
        partial_sum = jnp.dot(basis_rows.T, g, preferred_element_type=jnp.float32)
        outs.append(partial_sum)
    partial_sum = jnp.stack(outs, axis=1).astype(jnp.bfloat16)
    return lax.psum_scatter(partial_sum, "shard", scatter_dimension=0, tiled=True)


def solution(mesh):
    return jax.shard_map(
        body,
        mesh=mesh,
        in_specs=(P(None, "shard", "rep"), P()),
        out_specs=P("shard", None, "rep"),
        check_vma=False,
    )
```

```python
import jax
import jax.numpy as jnp
from jax import lax
from jax.experimental import pallas as pl
from jax.experimental.pallas import tpu as pltpu
from jax.sharding import PartitionSpec as P

RANK = 512
BLOCK = 128


def _mm(a, b, trans_b=False):
    dims = (((1,), (1,)), ((), ())) if trans_b else (((1,), (0,)), ((), ()))
    return lax.dot_general(a, b, dims, precision=lax.Precision.HIGHEST,
                           preferred_element_type=jnp.float32)


def _chol_inv_kernel(g_ref, w_ref, a_ref):
    n = g_ref.shape[0]
    b = BLOCK
    a_ref[...] = g_ref[...]
    rows = lax.broadcasted_iota(jnp.int32, (n, n), 0)
    cols = lax.broadcasted_iota(jnp.int32, (n, n), 1)
    w_ref[...] = jnp.where(rows == cols, 1.0, 0.0).astype(jnp.float32)
    arow = lax.broadcasted_iota(jnp.int32, (b, 2 * b), 0)
    acol = lax.broadcasted_iota(jnp.int32, (b, 2 * b), 1)
    bcol = lax.broadcasted_iota(jnp.int32, (b, b), 1)
    sub = lax.broadcasted_iota(jnp.int32, (b, 1), 0)
    eye = jnp.where(arow + b == acol, 1.0, 0.0).astype(jnp.float32)
    for p in range(n // b):
        lo = p * b
        blk = a_ref[lo:lo + b, lo:lo + b]
        aug = jnp.where(acol < b, jnp.concatenate([blk, blk], axis=1), eye)

        def step(k, aug):
            row = jnp.sum(jnp.where(arow == k, aug, 0.0), axis=0, keepdims=True)
            left = aug[:, :b]
            col = jnp.sum(jnp.where(bcol == k, left, 0.0), axis=1, keepdims=True)
            diag = jnp.sum(jnp.where(sub == k, col, 0.0), axis=0, keepdims=True)
            inv = 1.0 / jnp.sqrt(diag)
            lrow = row * inv
            strict = jnp.where(sub > k, col * inv, 0.0)
            upd = aug - strict * lrow
            return jnp.where((arow == k) & (acol >= b), lrow, upd)

        aug = lax.fori_loop(0, b, step, aug, unroll=4)
        winv = aug[:, b:]
        top = w_ref[lo:lo + b, :]
        newtop = _mm(winv, top)
        w_ref[lo:lo + b, :] = newtop
        hi = lo + b
        if hi < n:
            panel = _mm(a_ref[hi:, lo:lo + b], winv, trans_b=True)
            a_ref[hi:, hi:] = a_ref[hi:, hi:] - _mm(panel, panel, trans_b=True)
            w_ref[hi:, :] = w_ref[hi:, :] - _mm(panel, newtop)


def chol_inverse(gram):
    n = gram.shape[0]
    return pl.pallas_call(
        _chol_inv_kernel,
        out_shape=jax.ShapeDtypeStruct((n, n), jnp.float32),
        in_specs=[pl.BlockSpec(memory_space=pltpu.VMEM)],
        out_specs=pl.BlockSpec(memory_space=pltpu.VMEM),
        scratch_shapes=[pltpu.VMEM((n, n), jnp.float32)],
    )(gram)


mix_first = 668265263
mix_second = -2048144789
mix_third = -1028477387


def sketch_table(seeds, first_row, count, rank):
    rows = first_row + lax.iota(jnp.int32, count)
    columns = lax.iota(jnp.int32, rank)
    counter = rows[:, None] * jnp.int32(rank) + columns[None, :]
    hashed = jnp.bitwise_xor(counter[None, :, :], (seeds * jnp.int32(mix_first))[:, None, None])
    hashed = hashed * jnp.int32(mix_second)
    hashed = jnp.bitwise_xor(hashed, lax.shift_right_logical(hashed, jnp.int32(15)))
    hashed = hashed * jnp.int32(mix_third)
    hashed = jnp.bitwise_xor(hashed, lax.shift_right_logical(hashed, jnp.int32(13)))
    unit = lax.shift_right_logical(hashed, jnp.int32(8)).astype(jnp.float32) * (1.0 / 16777216.0)
    return (2.0 * unit - 1.0).astype(jnp.bfloat16)


def body(grads, seeds):
    mats, depth, width = grads.shape
    col0 = lax.axis_index("rep") * width
    outs = []
    for m in range(mats):
        table = sketch_table(seeds[m:m + 1], col0, width, RANK)[0]
        g = grads[m]
        partial = jnp.dot(g, table, preferred_element_type=jnp.float32)
        sketch_rows = lax.psum(partial, "rep")
        local_gram = jnp.dot(
            sketch_rows.T, sketch_rows,
            precision=lax.Precision.HIGHEST,
            preferred_element_type=jnp.float32,
        )
        gram = lax.psum(local_gram, "shard")
        inverse = chol_inverse(0.5 * (gram + gram.T))
        basis_rows = _mm(sketch_rows, inverse, trans_b=True).astype(jnp.bfloat16)
        partial_sum = jnp.dot(basis_rows.T, g, preferred_element_type=jnp.float32)
        outs.append(partial_sum)
    partial_sum = jnp.stack(outs, axis=1).astype(jnp.bfloat16)
    return lax.psum_scatter(partial_sum, "shard", scatter_dimension=0, tiled=True)


def solution(mesh):
    return jax.shard_map(
        body,
        mesh=mesh,
        in_specs=(P(None, "shard", "rep"), P()),
        out_specs=P("shard", None, "rep"),
        check_vma=False,
    )
```

```python
import jax
import jax.numpy as jnp
from jax import lax
from jax.experimental import pallas as pl
from jax.experimental.pallas import tpu as pltpu
from jax.sharding import PartitionSpec as P

RANK = 512
BLOCK = 128


def _mm(a, b, trans_b=False, precision=lax.Precision.HIGHEST):
    dims = (((1,), (1,)), ((), ())) if trans_b else (((1,), (0,)), ((), ()))
    return lax.dot_general(a, b, dims, precision=precision,
                           preferred_element_type=jnp.float32)


def _chol_inv_kernel(g_ref, w_ref, a_ref):
    n = g_ref.shape[0]
    b = BLOCK
    a_ref[...] = g_ref[...]
    rows = lax.broadcasted_iota(jnp.int32, (n, n), 0)
    cols = lax.broadcasted_iota(jnp.int32, (n, n), 1)
    w_ref[...] = jnp.where(rows == cols, 1.0, 0.0).astype(jnp.float32)
    arow = lax.broadcasted_iota(jnp.int32, (b, 2 * b), 0)
    acol = lax.broadcasted_iota(jnp.int32, (b, 2 * b), 1)
    bcol = lax.broadcasted_iota(jnp.int32, (b, b), 1)
    sub = lax.broadcasted_iota(jnp.int32, (b, 1), 0)
    eye = jnp.where(arow + b == acol, 1.0, 0.0).astype(jnp.float32)
    for p in range(n // b):
        lo = p * b
        blk = a_ref[lo:lo + b, lo:lo + b]
        aug = jnp.where(acol < b, jnp.concatenate([blk, blk], axis=1), eye)

        def step(k, aug):
            row = jnp.sum(jnp.where(arow == k, aug, 0.0), axis=0, keepdims=True)
            left = aug[:, :b]
            col = jnp.sum(jnp.where(bcol == k, left, 0.0), axis=1, keepdims=True)
            diag = jnp.sum(jnp.where(sub == k, col, 0.0), axis=0, keepdims=True)
            inv = 1.0 / jnp.sqrt(diag)
            lrow = row * inv
            strict = jnp.where(sub > k, col * inv, 0.0)
            upd = aug - strict * lrow
            return jnp.where((arow == k) & (acol >= b), lrow, upd)

        aug = lax.fori_loop(0, b, step, aug, unroll=4)
        winv = aug[:, b:]
        top = w_ref[lo:lo + b, :]
        newtop = _mm(winv, top)
        w_ref[lo:lo + b, :] = newtop
        hi = lo + b
        if hi < n:
            panel = _mm(a_ref[hi:, lo:lo + b], winv, trans_b=True)
            a_ref[hi:, hi:] = a_ref[hi:, hi:] - _mm(panel, panel, trans_b=True)
            w_ref[hi:, :] = w_ref[hi:, :] - _mm(panel, newtop)


def chol_inverse(gram):
    n = gram.shape[0]
    return pl.pallas_call(
        _chol_inv_kernel,
        out_shape=jax.ShapeDtypeStruct((n, n), jnp.float32),
        in_specs=[pl.BlockSpec(memory_space=pltpu.VMEM)],
        out_specs=pl.BlockSpec(memory_space=pltpu.VMEM),
        scratch_shapes=[pltpu.VMEM((n, n), jnp.float32)],
    )(gram)


mix_first = 668265263
mix_second = -2048144789
mix_third = -1028477387


def sketch_table(seeds, first_row, count, rank):
    rows = first_row + lax.iota(jnp.int32, count)
    columns = lax.iota(jnp.int32, rank)
    counter = rows[:, None] * jnp.int32(rank) + columns[None, :]
    hashed = jnp.bitwise_xor(counter[None, :, :], (seeds * jnp.int32(mix_first))[:, None, None])
    hashed = hashed * jnp.int32(mix_second)
    hashed = jnp.bitwise_xor(hashed, lax.shift_right_logical(hashed, jnp.int32(15)))
    hashed = hashed * jnp.int32(mix_third)
    hashed = jnp.bitwise_xor(hashed, lax.shift_right_logical(hashed, jnp.int32(13)))
    unit = lax.shift_right_logical(hashed, jnp.int32(8)).astype(jnp.float32) * (1.0 / 16777216.0)
    return (2.0 * unit - 1.0).astype(jnp.bfloat16)


def symmetric_psum(local, axis):
    b = BLOCK
    nb = local.shape[0] // b
    pairs = [(i, j) for i in range(nb) for j in range(i + 1)]
    packed = jnp.stack([local[i * b:(i + 1) * b, j * b:(j + 1) * b] for i, j in pairs])
    packed = lax.psum(packed, axis)
    blocks = {pair: packed[t] for t, pair in enumerate(pairs)}
    grid = []
    for i in range(nb):
        line = []
        for j in range(nb):
            if i == j:
                line.append(0.5 * (blocks[(i, i)] + blocks[(i, i)].T))
            elif i > j:
                line.append(blocks[(i, j)])
            else:
                line.append(blocks[(j, i)].T)
        grid.append(line)
    return jnp.block(grid)


def body(grads, seeds):
    mats, depth, width = grads.shape
    col0 = lax.axis_index("rep") * width
    outs = []
    for m in range(mats):
        table = sketch_table(seeds[m:m + 1], col0, width, RANK)[0]
        g = grads[m]
        partial = jnp.dot(g, table, preferred_element_type=jnp.float32)
        sketch_rows = lax.psum(partial, "rep")
        local_gram = jnp.dot(
            sketch_rows.T, sketch_rows,
            precision=lax.Precision.HIGHEST,
            preferred_element_type=jnp.float32,
        )
        gram = symmetric_psum(local_gram, "shard")
        inverse = chol_inverse(gram)
        basis_rows = _mm(
            sketch_rows, inverse, trans_b=True, precision=lax.Precision.HIGH
        ).astype(jnp.bfloat16)
        partial_sum = jnp.dot(basis_rows.T, g, preferred_element_type=jnp.float32)
        outs.append(partial_sum)
    partial_sum = jnp.stack(outs, axis=1).astype(jnp.bfloat16)
    return lax.psum_scatter(partial_sum, "shard", scatter_dimension=0, tiled=True)


def solution(mesh):
    return jax.shard_map(
        body,
        mesh=mesh,
        in_specs=(P(None, "shard", "rep"), P()),
        out_specs=P("shard", None, "rep"),
        check_vma=False,
    )
```

```python
import jax
import jax.numpy as jnp
from jax import lax
from jax.experimental import pallas as pl
from jax.experimental.pallas import tpu as pltpu
from jax.sharding import PartitionSpec as P

RANK = 512
BLOCK = 128


def _mm(a, b, trans_b=False, precision=lax.Precision.HIGHEST):
    dims = (((1,), (1,)), ((), ())) if trans_b else (((1,), (0,)), ((), ()))
    return lax.dot_general(a, b, dims, precision=precision,
                           preferred_element_type=jnp.float32)


def _tri(i, j):
    return i * (i + 1) // 2 + j


def _chol_inv_kernel(g_ref, w_ref, a_ref):
    b = BLOCK
    n = w_ref.shape[0]
    nb = n // b
    a_ref[...] = g_ref[...]
    for i in range(nb):
        d = g_ref[_tri(i, i)]
        a_ref[_tri(i, i)] = 0.5 * (d + d.T)
    rows = lax.broadcasted_iota(jnp.int32, (n, n), 0)
    cols = lax.broadcasted_iota(jnp.int32, (n, n), 1)
    w_ref[...] = jnp.where(rows == cols, 1.0, 0.0).astype(jnp.float32)
    arow = lax.broadcasted_iota(jnp.int32, (b, 2 * b), 0)
    acol = lax.broadcasted_iota(jnp.int32, (b, 2 * b), 1)
    bcol = lax.broadcasted_iota(jnp.int32, (b, b), 1)
    sub = lax.broadcasted_iota(jnp.int32, (b, 1), 0)
    eye = jnp.where(arow + b == acol, 1.0, 0.0).astype(jnp.float32)
    for p in range(nb):
        lo = p * b
        blk = a_ref[_tri(p, p)]
        aug = jnp.where(acol < b, jnp.concatenate([blk, blk], axis=1), eye)

        def step(k, aug):
            row = jnp.sum(jnp.where(arow == k, aug, 0.0), axis=0, keepdims=True)
            left = aug[:, :b]
            col = jnp.sum(jnp.where(bcol == k, left, 0.0), axis=1, keepdims=True)
            diag = jnp.sum(jnp.where(sub == k, col, 0.0), axis=0, keepdims=True)
            inv = 1.0 / jnp.sqrt(diag)
            lrow = row * inv
            strict = jnp.where(sub > k, col * inv, 0.0)
            upd = aug - strict * lrow
            return jnp.where((arow == k) & (acol >= b), lrow, upd)

        aug = lax.fori_loop(0, b, step, aug, unroll=4)
        winv = aug[:, b:]
        newtop = _mm(winv, w_ref[lo:lo + b, :])
        w_ref[lo:lo + b, :] = newtop
        panels = {i: _mm(a_ref[_tri(i, p)], winv, trans_b=True) for i in range(p + 1, nb)}
        for i in range(p + 1, nb):
            for j in range(p + 1, i + 1):
                a_ref[_tri(i, j)] = a_ref[_tri(i, j)] - _mm(panels[i], panels[j], trans_b=True)
            w_ref[i * b:(i + 1) * b, :] = w_ref[i * b:(i + 1) * b, :] - _mm(panels[i], newtop)


def chol_inverse(packed):
    t = packed.shape[0]
    nb = 1
    while nb * (nb + 1) // 2 < t:
        nb += 1
    n = nb * BLOCK
    return pl.pallas_call(
        _chol_inv_kernel,
        out_shape=jax.ShapeDtypeStruct((n, n), jnp.float32),
        in_specs=[pl.BlockSpec(memory_space=pltpu.VMEM)],
        out_specs=pl.BlockSpec(memory_space=pltpu.VMEM),
        scratch_shapes=[pltpu.VMEM(packed.shape, jnp.float32)],
    )(packed)


mix_first = 668265263
mix_second = -2048144789
mix_third = -1028477387


def sketch_table(seeds, first_row, count, rank):
    rows = first_row + lax.iota(jnp.int32, count)
    columns = lax.iota(jnp.int32, rank)
    counter = rows[:, None] * jnp.int32(rank) + columns[None, :]
    hashed = jnp.bitwise_xor(counter[None, :, :], (seeds * jnp.int32(mix_first))[:, None, None])
    hashed = hashed * jnp.int32(mix_second)
    hashed = jnp.bitwise_xor(hashed, lax.shift_right_logical(hashed, jnp.int32(15)))
    hashed = hashed * jnp.int32(mix_third)
    hashed = jnp.bitwise_xor(hashed, lax.shift_right_logical(hashed, jnp.int32(13)))
    unit = lax.shift_right_logical(hashed, jnp.int32(8)).astype(jnp.float32) * (1.0 / 16777216.0)
    return (2.0 * unit - 1.0).astype(jnp.bfloat16)


def lower_blocks_psum(local, axis):
    b = BLOCK
    nb = local.shape[0] // b
    pairs = [(i, j) for i in range(nb) for j in range(i + 1)]
    packed = jnp.stack([local[i * b:(i + 1) * b, j * b:(j + 1) * b] for i, j in pairs])
    return lax.psum(packed, axis)


def body(grads, seeds):
    mats, depth, width = grads.shape
    col0 = lax.axis_index("rep") * width
    outs = []
    for m in range(mats):
        table = sketch_table(seeds[m:m + 1], col0, width, RANK)[0]
        g = grads[m]
        partial = jnp.dot(g, table, preferred_element_type=jnp.float32)
        sketch_rows = lax.psum(partial, "rep")
        local_gram = jnp.dot(
            sketch_rows.T, sketch_rows,
            precision=lax.Precision.HIGH,
            preferred_element_type=jnp.float32,
        )
        gram = lower_blocks_psum(local_gram, "shard")
        inverse = chol_inverse(gram)
        basis_rows = _mm(
            sketch_rows, inverse, trans_b=True, precision=lax.Precision.HIGH
        ).astype(jnp.bfloat16)
        partial_sum = jnp.dot(basis_rows.T, g, preferred_element_type=jnp.float32)
        outs.append(partial_sum)
    partial_sum = jnp.stack(outs, axis=1).astype(jnp.bfloat16)
    return lax.psum_scatter(partial_sum, "shard", scatter_dimension=0, tiled=True)


def solution(mesh):
    return jax.shard_map(
        body,
        mesh=mesh,
        in_specs=(P(None, "shard", "rep"), P()),
        out_specs=P("shard", None, "rep"),
        check_vma=False,
    )
```

```python
import jax
import jax.numpy as jnp
from jax import lax
from jax.experimental import pallas as pl
from jax.experimental.pallas import tpu as pltpu
from jax.sharding import PartitionSpec as P

RANK = 512
BLOCK = 128


def _mm(a, b, trans_b=False, precision=lax.Precision.HIGHEST):
    dims = (((1,), (1,)), ((), ())) if trans_b else (((1,), (0,)), ((), ()))
    return lax.dot_general(a, b, dims, precision=precision,
                           preferred_element_type=jnp.float32)


def _tri(i, j):
    return i * (i + 1) // 2 + j


def _chol_inv_kernel(g_ref, w_ref, a_ref):
    b = BLOCK
    n = w_ref.shape[0]
    nb = n // b
    a_ref[...] = g_ref[...]
    for i in range(nb):
        d = g_ref[_tri(i, i)]
        a_ref[_tri(i, i)] = 0.5 * (d + d.T)
    rows = lax.broadcasted_iota(jnp.int32, (n, n), 0)
    cols = lax.broadcasted_iota(jnp.int32, (n, n), 1)
    w_ref[...] = jnp.where(rows == cols, 1.0, 0.0).astype(jnp.float32)
    arow = lax.broadcasted_iota(jnp.int32, (b, 2 * b), 0)
    acol = lax.broadcasted_iota(jnp.int32, (b, 2 * b), 1)
    bcol = lax.broadcasted_iota(jnp.int32, (b, b), 1)
    sub = lax.broadcasted_iota(jnp.int32, (b, 1), 0)
    eye = jnp.where(arow + b == acol, 1.0, 0.0).astype(jnp.float32)
    for p in range(nb):
        lo = p * b
        blk = a_ref[_tri(p, p)]
        aug = jnp.where(acol < b, jnp.concatenate([blk, blk], axis=1), eye)

        def step(k, aug):
            row = jnp.sum(jnp.where(arow == k, aug, 0.0), axis=0, keepdims=True)
            left = aug[:, :b]
            col = jnp.sum(jnp.where(bcol == k, left, 0.0), axis=1, keepdims=True)
            diag = jnp.sum(jnp.where(sub == k, col, 0.0), axis=0, keepdims=True)
            inv = lax.rsqrt(diag)
            inv = inv * (1.5 - 0.5 * diag * inv * inv)
            lrow = row * inv
            strict = jnp.where(sub > k, col * inv, 0.0)
            upd = aug - strict * lrow
            return jnp.where((arow == k) & (acol >= b), lrow, upd)

        aug = lax.fori_loop(0, b, step, aug, unroll=8)
        winv = aug[:, b:]
        newtop = _mm(winv, w_ref[lo:lo + b, :])
        w_ref[lo:lo + b, :] = newtop
        panels = {i: _mm(a_ref[_tri(i, p)], winv, trans_b=True) for i in range(p + 1, nb)}
        for i in range(p + 1, nb):
            for j in range(p + 1, i + 1):
                a_ref[_tri(i, j)] = a_ref[_tri(i, j)] - _mm(panels[i], panels[j], trans_b=True)
            w_ref[i * b:(i + 1) * b, :] = w_ref[i * b:(i + 1) * b, :] - _mm(panels[i], newtop)


def chol_inverse(packed):
    t = packed.shape[0]
    nb = 1
    while nb * (nb + 1) // 2 < t:
        nb += 1
    n = nb * BLOCK
    return pl.pallas_call(
        _chol_inv_kernel,
        out_shape=jax.ShapeDtypeStruct((n, n), jnp.float32),
        in_specs=[pl.BlockSpec(memory_space=pltpu.VMEM)],
        out_specs=pl.BlockSpec(memory_space=pltpu.VMEM),
        scratch_shapes=[pltpu.VMEM(packed.shape, jnp.float32)],
    )(packed)


mix_first = 668265263
mix_second = -2048144789
mix_third = -1028477387


def sketch_table(seeds, first_row, count, rank):
    rows = first_row + lax.iota(jnp.int32, count)
    columns = lax.iota(jnp.int32, rank)
    counter = rows[:, None] * jnp.int32(rank) + columns[None, :]
    hashed = jnp.bitwise_xor(counter[None, :, :], (seeds * jnp.int32(mix_first))[:, None, None])
    hashed = hashed * jnp.int32(mix_second)
    hashed = jnp.bitwise_xor(hashed, lax.shift_right_logical(hashed, jnp.int32(15)))
    hashed = hashed * jnp.int32(mix_third)
    hashed = jnp.bitwise_xor(hashed, lax.shift_right_logical(hashed, jnp.int32(13)))
    unit = lax.shift_right_logical(hashed, jnp.int32(8)).astype(jnp.float32) * (1.0 / 16777216.0)
    return (2.0 * unit - 1.0).astype(jnp.bfloat16)


def lower_blocks_psum(local, axis):
    b = BLOCK
    nb = local.shape[0] // b
    pairs = [(i, j) for i in range(nb) for j in range(i + 1)]
    packed = jnp.stack([local[i * b:(i + 1) * b, j * b:(j + 1) * b] for i, j in pairs])
    return lax.psum(packed, axis)


def body(grads, seeds):
    mats, depth, width = grads.shape
    col0 = lax.axis_index("rep") * width
    outs = []
    for m in range(mats):
        table = sketch_table(seeds[m:m + 1], col0, width, RANK)[0]
        g = grads[m]
        partial = jnp.dot(g, table, preferred_element_type=jnp.float32)
        sketch_rows = lax.psum(partial, "rep")
        local_gram = jnp.dot(
            sketch_rows.T, sketch_rows,
            precision=lax.Precision.HIGH,
            preferred_element_type=jnp.float32,
        )
        gram = lower_blocks_psum(local_gram, "shard")
        inverse = chol_inverse(gram)
        basis_rows = _mm(
            sketch_rows, inverse, trans_b=True, precision=lax.Precision.HIGH
        ).astype(jnp.bfloat16)
        partial_sum = jnp.dot(basis_rows.T, g, preferred_element_type=jnp.float32)
        outs.append(partial_sum)
    partial_sum = jnp.stack(outs, axis=1).astype(jnp.bfloat16)
    return lax.psum_scatter(partial_sum, "shard", scatter_dimension=0, tiled=True)


def solution(mesh):
    return jax.shard_map(
        body,
        mesh=mesh,
        in_specs=(P(None, "shard", "rep"), P()),
        out_specs=P("shard", None, "rep"),
        check_vma=False,
    )
```

```python
import jax
import jax.numpy as jnp
from jax import lax
from jax.experimental import pallas as pl
from jax.experimental.pallas import tpu as pltpu
from jax.sharding import PartitionSpec as P

RANK = 512
BLOCK = 128


def _mm(a, b, trans_b=False, precision=lax.Precision.HIGHEST):
    dims = (((1,), (1,)), ((), ())) if trans_b else (((1,), (0,)), ((), ()))
    return lax.dot_general(a, b, dims, precision=precision,
                           preferred_element_type=jnp.float32)


def _tri(i, j):
    return i * (i + 1) // 2 + j


def _chol_inv_kernel(g_ref, w_ref, a_ref):
    b = BLOCK
    n = w_ref.shape[0]
    nb = n // b
    a_ref[...] = g_ref[...]
    for i in range(nb):
        d = g_ref[_tri(i, i)]
        a_ref[_tri(i, i)] = 0.5 * (d + d.T)
    rows = lax.broadcasted_iota(jnp.int32, (n, n), 0)
    cols = lax.broadcasted_iota(jnp.int32, (n, n), 1)
    w_ref[...] = jnp.where(rows == cols, 1.0, 0.0).astype(jnp.float32)
    arow = lax.broadcasted_iota(jnp.int32, (b, 2 * b), 0)
    acol = lax.broadcasted_iota(jnp.int32, (b, 2 * b), 1)
    bcol = lax.broadcasted_iota(jnp.int32, (b, b), 1)
    sub = lax.broadcasted_iota(jnp.int32, (b, 1), 0)
    eye = jnp.where(arow + b == acol, 1.0, 0.0).astype(jnp.float32)
    for p in range(nb):
        lo = p * b
        blk = a_ref[_tri(p, p)]
        aug = jnp.where(acol < b, jnp.concatenate([blk, blk], axis=1), eye)

        def step(k, aug):
            row = jnp.sum(jnp.where(arow == k, aug, 0.0), axis=0, keepdims=True)
            left = aug[:, :b]
            col = jnp.sum(jnp.where(bcol == k, left, 0.0), axis=1, keepdims=True)
            diag = jnp.sum(jnp.where(sub == k, col, 0.0), axis=0, keepdims=True)
            inv = lax.rsqrt(diag)
            inv = inv * (1.5 - 0.5 * diag * inv * inv)
            lrow = row * inv
            strict = jnp.where(sub > k, col * inv, 0.0)
            upd = aug - strict * lrow
            return jnp.where((arow == k) & (acol >= b), lrow, upd)

        aug = lax.fori_loop(0, b, step, aug, unroll=8)
        winv = aug[:, b:]
        newtop = _mm(winv, w_ref[lo:lo + b, :])
        w_ref[lo:lo + b, :] = newtop
        panels = {i: _mm(a_ref[_tri(i, p)], winv, trans_b=True) for i in range(p + 1, nb)}
        for i in range(p + 1, nb):
            for j in range(p + 1, i + 1):
                a_ref[_tri(i, j)] = a_ref[_tri(i, j)] - _mm(panels[i], panels[j], trans_b=True)
            w_ref[i * b:(i + 1) * b, :] = w_ref[i * b:(i + 1) * b, :] - _mm(panels[i], newtop)


def chol_inverse(packed):
    t = packed.shape[0]
    nb = 1
    while nb * (nb + 1) // 2 < t:
        nb += 1
    n = nb * BLOCK
    return pl.pallas_call(
        _chol_inv_kernel,
        out_shape=jax.ShapeDtypeStruct((n, n), jnp.float32),
        in_specs=[pl.BlockSpec(memory_space=pltpu.VMEM)],
        out_specs=pl.BlockSpec(memory_space=pltpu.VMEM),
        scratch_shapes=[pltpu.VMEM(packed.shape, jnp.float32)],
    )(packed)


mix_first = 668265263
mix_second = -2048144789
mix_third = -1028477387


def sketch_table(seeds, first_row, count, rank):
    rows = first_row + lax.iota(jnp.int32, count)
    columns = lax.iota(jnp.int32, rank)
    counter = rows[:, None] * jnp.int32(rank) + columns[None, :]
    hashed = jnp.bitwise_xor(counter[None, :, :], (seeds * jnp.int32(mix_first))[:, None, None])
    hashed = hashed * jnp.int32(mix_second)
    hashed = jnp.bitwise_xor(hashed, lax.shift_right_logical(hashed, jnp.int32(15)))
    hashed = hashed * jnp.int32(mix_third)
    hashed = jnp.bitwise_xor(hashed, lax.shift_right_logical(hashed, jnp.int32(13)))
    unit = lax.shift_right_logical(hashed, jnp.int32(8)).astype(jnp.float32) * (1.0 / 16777216.0)
    return (2.0 * unit - 1.0).astype(jnp.bfloat16)


def lower_blocks_psum(local, axis):
    b = BLOCK
    nb = local.shape[0] // b
    pairs = [(i, j) for i in range(nb) for j in range(i + 1)]
    packed = jnp.stack([local[i * b:(i + 1) * b, j * b:(j + 1) * b] for i, j in pairs])
    return lax.psum(packed, axis)


def body(grads, seeds):
    mats, depth, width = grads.shape
    col0 = lax.axis_index("rep") * width
    outs = []
    for m in range(mats):
        table = sketch_table(seeds[m:m + 1], col0, width, RANK)[0]
        g = grads[m]
        partial = jnp.dot(g, table, preferred_element_type=jnp.float32)
        sketch_rows = lax.all_gather(
            lax.psum_scatter(partial, "rep", scatter_dimension=0, tiled=True),
            "rep", axis=0, tiled=True,
        )
        local_gram = jnp.dot(
            sketch_rows.T, sketch_rows,
            precision=lax.Precision.HIGH,
            preferred_element_type=jnp.float32,
        )
        gram = lower_blocks_psum(local_gram, "shard")
        inverse = chol_inverse(gram)
        basis_rows = _mm(
            sketch_rows, inverse, trans_b=True, precision=lax.Precision.HIGH
        ).astype(jnp.bfloat16)
        partial_sum = jnp.dot(basis_rows.T, g, preferred_element_type=jnp.float32)
        outs.append(partial_sum)
    partial_sum = jnp.stack(outs, axis=1).astype(jnp.bfloat16)
    return lax.psum_scatter(partial_sum, "shard", scatter_dimension=0, tiled=True)


def solution(mesh):
    return jax.shard_map(
        body,
        mesh=mesh,
        in_specs=(P(None, "shard", "rep"), P()),
        out_specs=P("shard", None, "rep"),
        check_vma=False,
    )
```

```python
import jax
import jax.numpy as jnp
from jax import lax
from jax.experimental import pallas as pl
from jax.experimental.pallas import tpu as pltpu
from jax.sharding import PartitionSpec as P

RANK = 512
BLOCK = 128
STAGES = 4


def _mm(a, b, trans_b=False, precision=lax.Precision.HIGHEST):
    dims = (((1,), (1,)), ((), ())) if trans_b else (((1,), (0,)), ((), ()))
    return lax.dot_general(a, b, dims, precision=precision,
                           preferred_element_type=jnp.float32)


def _tri(i, j):
    return i * (i + 1) // 2 + j


def _chol_inv_kernel(g_ref, w_ref, a_ref):
    b = BLOCK
    n = w_ref.shape[0]
    nb = n // b
    a_ref[...] = g_ref[...]
    for i in range(nb):
        d = g_ref[_tri(i, i)]
        a_ref[_tri(i, i)] = 0.5 * (d + d.T)
    rows = lax.broadcasted_iota(jnp.int32, (n, n), 0)
    cols = lax.broadcasted_iota(jnp.int32, (n, n), 1)
    w_ref[...] = jnp.where(rows == cols, 1.0, 0.0).astype(jnp.float32)
    arow = lax.broadcasted_iota(jnp.int32, (b, 2 * b), 0)
    acol = lax.broadcasted_iota(jnp.int32, (b, 2 * b), 1)
    bcol = lax.broadcasted_iota(jnp.int32, (b, b), 1)
    sub = lax.broadcasted_iota(jnp.int32, (b, 1), 0)
    eye = jnp.where(arow + b == acol, 1.0, 0.0).astype(jnp.float32)
    for p in range(nb):
        lo = p * b
        blk = a_ref[_tri(p, p)]
        aug = jnp.where(acol < b, jnp.concatenate([blk, blk], axis=1), eye)

        parts = []
        for q in range(STAGES):
            r0 = q * b // STAGES
            arow_q = arow[r0:]
            acol_q = acol[r0:]
            sub_q = sub[r0:]

            def step(k, low, arow_q=arow_q, acol_q=acol_q, sub_q=sub_q):
                row = jnp.sum(jnp.where(arow_q == k, low, 0.0), axis=0, keepdims=True)
                left = low[:, :b]
                col = jnp.sum(
                    jnp.where(bcol[:left.shape[0]] == k, left, 0.0), axis=1, keepdims=True
                )
                diag = jnp.sum(jnp.where(sub_q == k, col, 0.0), axis=0, keepdims=True)
                inv = lax.rsqrt(diag)
                inv = inv * (1.5 - 0.5 * diag * inv * inv)
                lrow = row * inv
                strict = jnp.where(sub_q > k, col * inv, 0.0)
                upd = low - strict * lrow
                return jnp.where((arow_q == k) & (acol_q >= b), lrow, upd)

            low = lax.fori_loop(r0, r0 + b // STAGES, step, aug[r0:], unroll=4)
            r1 = (q + 1) * b // STAGES
            parts.append(low[:r1 - r0])
            aug = jnp.concatenate(parts + ([low[r1 - r0:]] if q + 1 < STAGES else []), axis=0)
        winv = aug[:, b:]
        newtop = _mm(winv, w_ref[lo:lo + b, :])
        w_ref[lo:lo + b, :] = newtop
        panels = {i: _mm(a_ref[_tri(i, p)], winv, trans_b=True) for i in range(p + 1, nb)}
        for i in range(p + 1, nb):
            for j in range(p + 1, i + 1):
                a_ref[_tri(i, j)] = a_ref[_tri(i, j)] - _mm(panels[i], panels[j], trans_b=True)
            w_ref[i * b:(i + 1) * b, :] = w_ref[i * b:(i + 1) * b, :] - _mm(panels[i], newtop)


def chol_inverse(packed):
    t = packed.shape[0]
    nb = 1
    while nb * (nb + 1) // 2 < t:
        nb += 1
    n = nb * BLOCK
    return pl.pallas_call(
        _chol_inv_kernel,
        out_shape=jax.ShapeDtypeStruct((n, n), jnp.float32),
        in_specs=[pl.BlockSpec(memory_space=pltpu.VMEM)],
        out_specs=pl.BlockSpec(memory_space=pltpu.VMEM),
        scratch_shapes=[pltpu.VMEM(packed.shape, jnp.float32)],
    )(packed)


mix_first = 668265263
mix_second = -2048144789
mix_third = -1028477387


def sketch_table(seeds, first_row, count, rank):
    rows = first_row + lax.iota(jnp.int32, count)
    columns = lax.iota(jnp.int32, rank)
    counter = rows[:, None] * jnp.int32(rank) + columns[None, :]
    hashed = jnp.bitwise_xor(counter[None, :, :], (seeds * jnp.int32(mix_first))[:, None, None])
    hashed = hashed * jnp.int32(mix_second)
    hashed = jnp.bitwise_xor(hashed, lax.shift_right_logical(hashed, jnp.int32(15)))
    hashed = hashed * jnp.int32(mix_third)
    hashed = jnp.bitwise_xor(hashed, lax.shift_right_logical(hashed, jnp.int32(13)))
    unit = lax.shift_right_logical(hashed, jnp.int32(8)).astype(jnp.float32) * (1.0 / 16777216.0)
    return (2.0 * unit - 1.0).astype(jnp.bfloat16)


def lower_blocks_psum(local, axis):
    b = BLOCK
    nb = local.shape[0] // b
    pairs = [(i, j) for i in range(nb) for j in range(i + 1)]
    packed = jnp.stack([local[i * b:(i + 1) * b, j * b:(j + 1) * b] for i, j in pairs])
    return lax.psum(packed, axis)


def body(grads, seeds):
    mats, depth, width = grads.shape
    col0 = lax.axis_index("rep") * width
    outs = []
    for m in range(mats):
        table = sketch_table(seeds[m:m + 1], col0, width, RANK)[0]
        g = grads[m]
        partial = jnp.dot(g, table, preferred_element_type=jnp.float32)
        sketch_rows = lax.psum(partial, "rep")
        local_gram = jnp.dot(
            sketch_rows.T, sketch_rows,
            precision=lax.Precision.HIGH,
            preferred_element_type=jnp.float32,
        )
        gram = lower_blocks_psum(local_gram, "shard")
        inverse = chol_inverse(gram)
        basis_rows = _mm(
            sketch_rows, inverse, trans_b=True, precision=lax.Precision.HIGH
        ).astype(jnp.bfloat16)
        partial_sum = jnp.dot(basis_rows.T, g, preferred_element_type=jnp.float32)
        outs.append(partial_sum)
    partial_sum = jnp.stack(outs, axis=1).astype(jnp.bfloat16)
    return lax.psum_scatter(partial_sum, "shard", scatter_dimension=0, tiled=True)


def solution(mesh):
    return jax.shard_map(
        body,
        mesh=mesh,
        in_specs=(P(None, "shard", "rep"), P()),
        out_specs=P("shard", None, "rep"),
        check_vma=False,
    )
```

```python
import jax
import jax.numpy as jnp
from jax import lax
from jax.experimental import pallas as pl
from jax.experimental.pallas import tpu as pltpu
from jax.sharding import PartitionSpec as P

RANK = 512
BLOCK = 128
STAGES = 4


def _mm(a, b, trans_b=False, precision=lax.Precision.HIGHEST):
    dims = (((1,), (1,)), ((), ())) if trans_b else (((1,), (0,)), ((), ()))
    return lax.dot_general(a, b, dims, precision=precision,
                           preferred_element_type=jnp.float32)


def _tri(i, j):
    return i * (i + 1) // 2 + j


def _chol_inv_kernel(g_ref, w_ref, a_ref):
    b = BLOCK
    n = w_ref.shape[0]
    nb = n // b
    a_ref[...] = g_ref[...]
    for i in range(nb):
        d = g_ref[_tri(i, i)]
        a_ref[_tri(i, i)] = 0.5 * (d + d.T)
    rows = lax.broadcasted_iota(jnp.int32, (n, n), 0)
    cols = lax.broadcasted_iota(jnp.int32, (n, n), 1)
    w_ref[...] = jnp.where(rows == cols, 1.0, 0.0).astype(jnp.float32)
    arow = lax.broadcasted_iota(jnp.int32, (b, 2 * b), 0)
    acol = lax.broadcasted_iota(jnp.int32, (b, 2 * b), 1)
    bcol = lax.broadcasted_iota(jnp.int32, (b, b), 1)
    sub = lax.broadcasted_iota(jnp.int32, (b, 1), 0)
    eye = jnp.where(arow + b == acol, 1.0, 0.0).astype(jnp.float32)
    for p in range(nb):
        lo = p * b
        blk = a_ref[_tri(p, p)]
        aug = jnp.where(acol < b, jnp.concatenate([blk, blk], axis=1), eye)

        parts = []
        for q in range(STAGES):
            r0 = q * b // STAGES
            arow_q = arow[r0:]
            acol_q = acol[r0:]
            sub_q = sub[r0:]

            def step(k, low, arow_q=arow_q, acol_q=acol_q, sub_q=sub_q):
                row = jnp.sum(jnp.where(arow_q == k, low, 0.0), axis=0, keepdims=True)
                left = low[:, :b]
                col = jnp.sum(
                    jnp.where(bcol[:left.shape[0]] == k, left, 0.0), axis=1, keepdims=True
                )
                diag = jnp.sum(jnp.where(sub_q == k, col, 0.0), axis=0, keepdims=True)
                inv = lax.rsqrt(diag)
                inv = inv * (1.5 - 0.5 * diag * inv * inv)
                lrow = row * inv
                strict = jnp.where(sub_q > k, col * inv, 0.0)
                upd = low - strict * lrow
                return jnp.where((arow_q == k) & (acol_q >= b), lrow, upd)

            low = lax.fori_loop(r0, r0 + b // STAGES, step, aug[r0:], unroll=2)
            r1 = (q + 1) * b // STAGES
            parts.append(low[:r1 - r0])
            aug = jnp.concatenate(parts + ([low[r1 - r0:]] if q + 1 < STAGES else []), axis=0)
        winv = aug[:, b:]
        newtop = _mm(winv, w_ref[lo:lo + b, :])
        w_ref[lo:lo + b, :] = newtop
        panels = {i: _mm(a_ref[_tri(i, p)], winv, trans_b=True) for i in range(p + 1, nb)}
        for i in range(p + 1, nb):
            for j in range(p + 1, i + 1):
                a_ref[_tri(i, j)] = a_ref[_tri(i, j)] - _mm(panels[i], panels[j], trans_b=True)
            w_ref[i * b:(i + 1) * b, :] = w_ref[i * b:(i + 1) * b, :] - _mm(panels[i], newtop)


def chol_inverse(packed):
    t = packed.shape[0]
    nb = 1
    while nb * (nb + 1) // 2 < t:
        nb += 1
    n = nb * BLOCK
    return pl.pallas_call(
        _chol_inv_kernel,
        out_shape=jax.ShapeDtypeStruct((n, n), jnp.float32),
        in_specs=[pl.BlockSpec(memory_space=pltpu.VMEM)],
        out_specs=pl.BlockSpec(memory_space=pltpu.VMEM),
        scratch_shapes=[pltpu.VMEM(packed.shape, jnp.float32)],
    )(packed)


mix_first = 668265263
mix_second = -2048144789
mix_third = -1028477387


def sketch_table(seeds, first_row, count, rank):
    rows = first_row + lax.iota(jnp.int32, count)
    columns = lax.iota(jnp.int32, rank)
    counter = rows[:, None] * jnp.int32(rank) + columns[None, :]
    hashed = jnp.bitwise_xor(counter[None, :, :], (seeds * jnp.int32(mix_first))[:, None, None])
    hashed = hashed * jnp.int32(mix_second)
    hashed = jnp.bitwise_xor(hashed, lax.shift_right_logical(hashed, jnp.int32(15)))
    hashed = hashed * jnp.int32(mix_third)
    hashed = jnp.bitwise_xor(hashed, lax.shift_right_logical(hashed, jnp.int32(13)))
    unit = lax.shift_right_logical(hashed, jnp.int32(8)).astype(jnp.float32) * (1.0 / 16777216.0)
    return (2.0 * unit - 1.0).astype(jnp.bfloat16)


def lower_blocks_psum(local, axis):
    b = BLOCK
    nb = local.shape[0] // b
    pairs = [(i, j) for i in range(nb) for j in range(i + 1)]
    packed = jnp.stack([local[i * b:(i + 1) * b, j * b:(j + 1) * b] for i, j in pairs])
    return lax.psum(packed, axis)


def body(grads, seeds):
    mats, depth, width = grads.shape
    col0 = lax.axis_index("rep") * width
    outs = []
    for m in range(mats):
        table = sketch_table(seeds[m:m + 1], col0, width, RANK)[0]
        g = grads[m]
        partial = jnp.dot(g, table, preferred_element_type=jnp.float32)
        sketch_rows = lax.psum(partial, "rep")
        local_gram = jnp.dot(
            sketch_rows.T, sketch_rows,
            precision=lax.Precision.HIGHEST,
            preferred_element_type=jnp.float32,
        )
        gram = lower_blocks_psum(local_gram, "shard")
        inverse = chol_inverse(gram)
        basis_rows = _mm(sketch_rows, inverse, trans_b=True).astype(jnp.bfloat16)
        partial_sum = jnp.dot(basis_rows.T, g, preferred_element_type=jnp.float32)
        outs.append(partial_sum)
    partial_sum = jnp.stack(outs, axis=1).astype(jnp.bfloat16)
    return lax.psum_scatter(partial_sum, "shard", scatter_dimension=0, tiled=True)


def solution(mesh):
    return jax.shard_map(
        body,
        mesh=mesh,
        in_specs=(P(None, "shard", "rep"), P()),
        out_specs=P("shard", None, "rep"),
        check_vma=False,
    )
```

```python
import jax
import jax.numpy as jnp
from jax import lax
from jax.experimental import pallas as pl
from jax.experimental.pallas import tpu as pltpu
from jax.sharding import PartitionSpec as P

RANK = 512
BLOCK = 128
STAGES = 8


def _mm(a, b, trans_b=False, precision=lax.Precision.HIGHEST):
    dims = (((1,), (1,)), ((), ())) if trans_b else (((1,), (0,)), ((), ()))
    return lax.dot_general(a, b, dims, precision=precision,
                           preferred_element_type=jnp.float32)


def _tri(i, j):
    return i * (i + 1) // 2 + j


def _chol_inv_kernel(g_ref, w_ref, a_ref):
    b = BLOCK
    n = w_ref.shape[0]
    nb = n // b
    a_ref[...] = g_ref[...]
    for i in range(nb):
        d = g_ref[_tri(i, i)]
        a_ref[_tri(i, i)] = 0.5 * (d + d.T)
    rows = lax.broadcasted_iota(jnp.int32, (n, n), 0)
    cols = lax.broadcasted_iota(jnp.int32, (n, n), 1)
    w_ref[...] = jnp.where(rows == cols, 1.0, 0.0).astype(jnp.float32)
    arow = lax.broadcasted_iota(jnp.int32, (b, 2 * b), 0)
    acol = lax.broadcasted_iota(jnp.int32, (b, 2 * b), 1)
    bcol = lax.broadcasted_iota(jnp.int32, (b, b), 1)
    sub = lax.broadcasted_iota(jnp.int32, (b, 1), 0)
    eye = jnp.where(arow + b == acol, 1.0, 0.0).astype(jnp.float32)
    for p in range(nb):
        lo = p * b
        blk = a_ref[_tri(p, p)]
        aug = jnp.where(acol < b, jnp.concatenate([blk, blk], axis=1), eye)

        parts = []
        for q in range(STAGES):
            r0 = q * b // STAGES
            arow_q = arow[r0:]
            acol_q = acol[r0:]
            sub_q = sub[r0:]

            def step(k, low, arow_q=arow_q, acol_q=acol_q, sub_q=sub_q):
                row = jnp.sum(jnp.where(arow_q == k, low, 0.0), axis=0, keepdims=True)
                left = low[:, :b]
                col = jnp.sum(
                    jnp.where(bcol[:left.shape[0]] == k, left, 0.0), axis=1, keepdims=True
                )
                diag = jnp.sum(jnp.where(sub_q == k, col, 0.0), axis=0, keepdims=True)
                inv = lax.rsqrt(diag)
                inv = inv * (1.5 - 0.5 * diag * inv * inv)
                lrow = row * inv
                strict = jnp.where(sub_q > k, col * inv, 0.0)
                upd = low - strict * lrow
                return jnp.where((arow_q == k) & (acol_q >= b), lrow, upd)

            low = lax.fori_loop(r0, r0 + b // STAGES, step, aug[r0:], unroll=1)
            r1 = (q + 1) * b // STAGES
            parts.append(low[:r1 - r0])
            aug = jnp.concatenate(parts + ([low[r1 - r0:]] if q + 1 < STAGES else []), axis=0)
        winv = aug[:, b:]
        newtop = _mm(winv, w_ref[lo:lo + b, :])
        w_ref[lo:lo + b, :] = newtop
        panels = {i: _mm(a_ref[_tri(i, p)], winv, trans_b=True) for i in range(p + 1, nb)}
        for i in range(p + 1, nb):
            for j in range(p + 1, i + 1):
                a_ref[_tri(i, j)] = a_ref[_tri(i, j)] - _mm(panels[i], panels[j], trans_b=True)
            w_ref[i * b:(i + 1) * b, :] = w_ref[i * b:(i + 1) * b, :] - _mm(panels[i], newtop)


def chol_inverse(packed):
    t = packed.shape[0]
    nb = 1
    while nb * (nb + 1) // 2 < t:
        nb += 1
    n = nb * BLOCK
    return pl.pallas_call(
        _chol_inv_kernel,
        out_shape=jax.ShapeDtypeStruct((n, n), jnp.float32),
        in_specs=[pl.BlockSpec(memory_space=pltpu.VMEM)],
        out_specs=pl.BlockSpec(memory_space=pltpu.VMEM),
        scratch_shapes=[pltpu.VMEM(packed.shape, jnp.float32)],
    )(packed)


mix_first = 668265263
mix_second = -2048144789
mix_third = -1028477387


def sketch_table(seeds, first_row, count, rank):
    rows = first_row + lax.iota(jnp.int32, count)
    columns = lax.iota(jnp.int32, rank)
    counter = rows[:, None] * jnp.int32(rank) + columns[None, :]
    hashed = jnp.bitwise_xor(counter[None, :, :], (seeds * jnp.int32(mix_first))[:, None, None])
    hashed = hashed * jnp.int32(mix_second)
    hashed = jnp.bitwise_xor(hashed, lax.shift_right_logical(hashed, jnp.int32(15)))
    hashed = hashed * jnp.int32(mix_third)
    hashed = jnp.bitwise_xor(hashed, lax.shift_right_logical(hashed, jnp.int32(13)))
    unit = lax.shift_right_logical(hashed, jnp.int32(8)).astype(jnp.float32) * (1.0 / 16777216.0)
    return (2.0 * unit - 1.0).astype(jnp.bfloat16)


def lower_blocks_psum(local, axis):
    b = BLOCK
    nb = local.shape[0] // b
    pairs = [(i, j) for i in range(nb) for j in range(i + 1)]
    packed = jnp.stack([local[i * b:(i + 1) * b, j * b:(j + 1) * b] for i, j in pairs])
    return lax.psum(packed, axis)


def body(grads, seeds):
    mats, depth, width = grads.shape
    col0 = lax.axis_index("rep") * width
    outs = []
    for m in range(mats):
        table = sketch_table(seeds[m:m + 1], col0, width, RANK)[0]
        g = grads[m]
        partial = jnp.dot(g, table, preferred_element_type=jnp.float32)
        sketch_rows = lax.psum(partial, "rep")
        local_gram = jnp.dot(
            sketch_rows.T, sketch_rows,
            precision=lax.Precision.HIGHEST,
            preferred_element_type=jnp.float32,
        )
        gram = lower_blocks_psum(local_gram, "shard")
        inverse = chol_inverse(gram)
        basis_rows = _mm(sketch_rows, inverse, trans_b=True).astype(jnp.bfloat16)
        partial_sum = jnp.dot(basis_rows.T, g, preferred_element_type=jnp.float32)
        outs.append(partial_sum)
    partial_sum = jnp.stack(outs, axis=1).astype(jnp.bfloat16)
    return lax.psum_scatter(partial_sum, "shard", scatter_dimension=0, tiled=True)


def solution(mesh):
    return jax.shard_map(
        body,
        mesh=mesh,
        in_specs=(P(None, "shard", "rep"), P()),
        out_specs=P("shard", None, "rep"),
        check_vma=False,
    )
```

```python
import jax
import jax.numpy as jnp
from jax import lax
from jax.experimental import pallas as pl
from jax.experimental.pallas import tpu as pltpu
from jax.sharding import PartitionSpec as P

RANK = 512
BLOCK = 128
STAGES = 4


def _mm(a, b, trans_b=False, precision=lax.Precision.HIGHEST):
    dims = (((1,), (1,)), ((), ())) if trans_b else (((1,), (0,)), ((), ()))
    return lax.dot_general(a, b, dims, precision=precision,
                           preferred_element_type=jnp.float32)


def _tri(i, j):
    return i * (i + 1) // 2 + j


def _chol_inv_kernel(g_ref, w_ref, a_ref):
    b = BLOCK
    n = w_ref.shape[0]
    nb = n // b
    a_ref[...] = g_ref[...]
    for i in range(nb):
        d = g_ref[_tri(i, i)]
        a_ref[_tri(i, i)] = 0.5 * (d + d.T)
    rows = lax.broadcasted_iota(jnp.int32, (n, n), 0)
    cols = lax.broadcasted_iota(jnp.int32, (n, n), 1)
    w_ref[...] = jnp.where(rows == cols, 1.0, 0.0).astype(jnp.float32)
    arow = lax.broadcasted_iota(jnp.int32, (b, 2 * b), 0)
    acol = lax.broadcasted_iota(jnp.int32, (b, 2 * b), 1)
    bcol = lax.broadcasted_iota(jnp.int32, (b, b), 1)
    sub = lax.broadcasted_iota(jnp.int32, (b, 1), 0)
    eye = jnp.where(arow + b == acol, 1.0, 0.0).astype(jnp.float32)
    for p in range(nb):
        lo = p * b
        blk = a_ref[_tri(p, p)]
        aug = jnp.where(acol < b, jnp.concatenate([blk, blk], axis=1), eye)

        parts = []
        for q in range(STAGES):
            r0 = q * b // STAGES
            arow_q = arow[r0:]
            acol_q = acol[r0:]
            sub_q = sub[r0:]

            def step(k, low, arow_q=arow_q, acol_q=acol_q, sub_q=sub_q):
                row = jnp.sum(jnp.where(arow_q == k, low, 0.0), axis=0, keepdims=True)
                left = low[:, :b]
                col = jnp.sum(
                    jnp.where(bcol[:left.shape[0]] == k, left, 0.0), axis=1, keepdims=True
                )
                diag = jnp.sum(jnp.where(sub_q == k, col, 0.0), axis=0, keepdims=True)
                inv = lax.rsqrt(diag)
                inv = inv * (1.5 - 0.5 * diag * inv * inv)
                lrow = row * inv
                strict = jnp.where(sub_q > k, col * inv, 0.0)
                upd = low - strict * lrow
                return jnp.where((arow_q == k) & (acol_q >= b), lrow, upd)

            low = lax.fori_loop(r0, r0 + b // STAGES, step, aug[r0:], unroll=2)
            r1 = (q + 1) * b // STAGES
            parts.append(low[:r1 - r0])
            aug = jnp.concatenate(parts + ([low[r1 - r0:]] if q + 1 < STAGES else []), axis=0)
        winv = aug[:, b:]
        hi = lo + b
        newtop = _mm(winv, w_ref[lo:lo + b, :hi])
        w_ref[lo:lo + b, :hi] = newtop
        panels = {i: _mm(a_ref[_tri(i, p)], winv, trans_b=True) for i in range(p + 1, nb)}
        for i in range(p + 1, nb):
            for j in range(p + 1, i + 1):
                a_ref[_tri(i, j)] = a_ref[_tri(i, j)] - _mm(panels[i], panels[j], trans_b=True)
            w_ref[i * b:(i + 1) * b, :hi] = w_ref[i * b:(i + 1) * b, :hi] - _mm(panels[i], newtop)


def chol_inverse(packed):
    t = packed.shape[0]
    nb = 1
    while nb * (nb + 1) // 2 < t:
        nb += 1
    n = nb * BLOCK
    return pl.pallas_call(
        _chol_inv_kernel,
        out_shape=jax.ShapeDtypeStruct((n, n), jnp.float32),
        in_specs=[pl.BlockSpec(memory_space=pltpu.VMEM)],
        out_specs=pl.BlockSpec(memory_space=pltpu.VMEM),
        scratch_shapes=[pltpu.VMEM(packed.shape, jnp.float32)],
    )(packed)


mix_first = 668265263
mix_second = -2048144789
mix_third = -1028477387


def sketch_table(seeds, first_row, count, rank):
    rows = first_row + lax.iota(jnp.int32, count)
    columns = lax.iota(jnp.int32, rank)
    counter = rows[:, None] * jnp.int32(rank) + columns[None, :]
    hashed = jnp.bitwise_xor(counter[None, :, :], (seeds * jnp.int32(mix_first))[:, None, None])
    hashed = hashed * jnp.int32(mix_second)
    hashed = jnp.bitwise_xor(hashed, lax.shift_right_logical(hashed, jnp.int32(15)))
    hashed = hashed * jnp.int32(mix_third)
    hashed = jnp.bitwise_xor(hashed, lax.shift_right_logical(hashed, jnp.int32(13)))
    unit = lax.shift_right_logical(hashed, jnp.int32(8)).astype(jnp.float32) * (1.0 / 16777216.0)
    return (2.0 * unit - 1.0).astype(jnp.bfloat16)


def lower_blocks_psum(local, axis):
    b = BLOCK
    nb = local.shape[0] // b
    pairs = [(i, j) for i in range(nb) for j in range(i + 1)]
    packed = jnp.stack([local[i * b:(i + 1) * b, j * b:(j + 1) * b] for i, j in pairs])
    return lax.psum(packed, axis)


def body(grads, seeds):
    mats, depth, width = grads.shape
    col0 = lax.axis_index("rep") * width
    outs = []
    for m in range(mats):
        table = sketch_table(seeds[m:m + 1], col0, width, RANK)[0]
        g = grads[m]
        partial = jnp.dot(g, table, preferred_element_type=jnp.float32)
        sketch_rows = lax.psum(partial, "rep")
        local_gram = jnp.dot(
            sketch_rows.T, sketch_rows,
            precision=lax.Precision.HIGHEST,
            preferred_element_type=jnp.float32,
        )
        gram = lower_blocks_psum(local_gram, "shard")
        inverse = chol_inverse(gram)
        basis_rows = _mm(sketch_rows, inverse, trans_b=True).astype(jnp.bfloat16)
        partial_sum = jnp.dot(basis_rows.T, g, preferred_element_type=jnp.float32)
        outs.append(partial_sum)
    partial_sum = jnp.stack(outs, axis=1).astype(jnp.bfloat16)
    return lax.psum_scatter(partial_sum, "shard", scatter_dimension=0, tiled=True)


def solution(mesh):
    return jax.shard_map(
        body,
        mesh=mesh,
        in_specs=(P(None, "shard", "rep"), P()),
        out_specs=P("shard", None, "rep"),
        check_vma=False,
    )
```

```python
import jax
import jax.numpy as jnp
from jax import lax
from jax.experimental import pallas as pl
from jax.experimental.pallas import tpu as pltpu
from jax.sharding import PartitionSpec as P

RANK = 512
BLOCK = 128
STAGES = 4


def _mm(a, b, trans_b=False, precision=lax.Precision.HIGHEST):
    dims = (((1,), (1,)), ((), ())) if trans_b else (((1,), (0,)), ((), ()))
    return lax.dot_general(a, b, dims, precision=precision,
                           preferred_element_type=jnp.float32)


def _tri(i, j):
    return i * (i + 1) // 2 + j


def _chol_inv_kernel(g_ref, w_ref, a_ref):
    b = BLOCK
    n = w_ref.shape[0]
    nb = n // b
    a_ref[...] = g_ref[...]
    for i in range(nb):
        d = g_ref[_tri(i, i)]
        a_ref[_tri(i, i)] = 0.5 * (d + d.T)
    rows = lax.broadcasted_iota(jnp.int32, (n, n), 0)
    cols = lax.broadcasted_iota(jnp.int32, (n, n), 1)
    w_ref[...] = jnp.where(rows == cols, 1.0, 0.0).astype(jnp.float32)
    arow = lax.broadcasted_iota(jnp.int32, (b, 2 * b), 0)
    acol = lax.broadcasted_iota(jnp.int32, (b, 2 * b), 1)
    bcol = lax.broadcasted_iota(jnp.int32, (b, b), 1)
    sub = lax.broadcasted_iota(jnp.int32, (b, 1), 0)
    eye = jnp.where(arow + b == acol, 1.0, 0.0).astype(jnp.float32)
    for p in range(nb):
        lo = p * b
        blk = a_ref[_tri(p, p)]
        aug = jnp.where(acol < b, jnp.concatenate([blk, blk], axis=1), eye)

        parts = []
        for q in range(STAGES):
            r0 = q * b // STAGES
            arow_q = arow[r0:]
            acol_q = acol[r0:]
            sub_q = sub[r0:]

            def step(k, low, arow_q=arow_q, acol_q=acol_q, sub_q=sub_q):
                row = jnp.sum(jnp.where(arow_q == k, low, 0.0), axis=0, keepdims=True)
                left = low[:, :b]
                col = jnp.sum(
                    jnp.where(bcol[:left.shape[0]] == k, left, 0.0), axis=1, keepdims=True
                )
                diag = jnp.sum(jnp.where(sub_q == k, col, 0.0), axis=0, keepdims=True)
                inv = lax.rsqrt(diag)
                inv = inv * (1.5 - 0.5 * diag * inv * inv)
                lrow = row * inv
                strict = jnp.where(sub_q > k, col * inv, 0.0)
                upd = low - strict * lrow
                return jnp.where((arow_q == k) & (acol_q >= b), lrow, upd)

            low = lax.fori_loop(r0, r0 + b // STAGES, step, aug[r0:], unroll=4)
            r1 = (q + 1) * b // STAGES
            parts.append(low[:r1 - r0])
            aug = jnp.concatenate(parts + ([low[r1 - r0:]] if q + 1 < STAGES else []), axis=0)
        winv = aug[:, b:]
        hi = lo + b
        newtop = _mm(winv, w_ref[lo:lo + b, :hi])
        w_ref[lo:lo + b, :hi] = newtop
        panels = {i: _mm(a_ref[_tri(i, p)], winv, trans_b=True) for i in range(p + 1, nb)}
        for i in range(p + 1, nb):
            for j in range(p + 1, i + 1):
                a_ref[_tri(i, j)] = a_ref[_tri(i, j)] - _mm(panels[i], panels[j], trans_b=True)
            w_ref[i * b:(i + 1) * b, :hi] = w_ref[i * b:(i + 1) * b, :hi] - _mm(panels[i], newtop)


def chol_inverse(packed):
    t = packed.shape[0]
    nb = 1
    while nb * (nb + 1) // 2 < t:
        nb += 1
    n = nb * BLOCK
    return pl.pallas_call(
        _chol_inv_kernel,
        out_shape=jax.ShapeDtypeStruct((n, n), jnp.float32),
        in_specs=[pl.BlockSpec(memory_space=pltpu.VMEM)],
        out_specs=pl.BlockSpec(memory_space=pltpu.VMEM),
        scratch_shapes=[pltpu.VMEM(packed.shape, jnp.float32)],
    )(packed)


mix_first = 668265263
mix_second = -2048144789
mix_third = -1028477387


def sketch_table(seeds, first_row, count, rank):
    rows = first_row + lax.iota(jnp.int32, count)
    columns = lax.iota(jnp.int32, rank)
    counter = rows[:, None] * jnp.int32(rank) + columns[None, :]
    hashed = jnp.bitwise_xor(counter[None, :, :], (seeds * jnp.int32(mix_first))[:, None, None])
    hashed = hashed * jnp.int32(mix_second)
    hashed = jnp.bitwise_xor(hashed, lax.shift_right_logical(hashed, jnp.int32(15)))
    hashed = hashed * jnp.int32(mix_third)
    hashed = jnp.bitwise_xor(hashed, lax.shift_right_logical(hashed, jnp.int32(13)))
    unit = lax.shift_right_logical(hashed, jnp.int32(8)).astype(jnp.float32) * (1.0 / 16777216.0)
    return (2.0 * unit - 1.0).astype(jnp.bfloat16)


def lower_blocks_psum(local, axis):
    b = BLOCK
    nb = local.shape[0] // b
    pairs = [(i, j) for i in range(nb) for j in range(i + 1)]
    packed = jnp.stack([local[i * b:(i + 1) * b, j * b:(j + 1) * b] for i, j in pairs])
    return lax.psum(packed, axis)


def body(grads, seeds):
    mats, depth, width = grads.shape
    col0 = lax.axis_index("rep") * width
    outs = []
    for m in range(mats):
        table = sketch_table(seeds[m:m + 1], col0, width, RANK)[0]
        g = grads[m]
        partial = jnp.dot(g, table, preferred_element_type=jnp.float32)
        sketch_rows = lax.psum(partial, "rep")
        local_gram = jnp.dot(
            sketch_rows.T, sketch_rows,
            precision=lax.Precision.HIGHEST,
            preferred_element_type=jnp.float32,
        )
        gram = lower_blocks_psum(local_gram, "shard")
        inverse = chol_inverse(gram)
        basis_rows = _mm(sketch_rows, inverse, trans_b=True).astype(jnp.bfloat16)
        partial_sum = jnp.dot(basis_rows.T, g, preferred_element_type=jnp.float32)
        outs.append(partial_sum)
    partial_sum = jnp.stack(outs, axis=1).astype(jnp.bfloat16)
    return lax.psum_scatter(partial_sum, "shard", scatter_dimension=0, tiled=True)


def solution(mesh):
    return jax.shard_map(
        body,
        mesh=mesh,
        in_specs=(P(None, "shard", "rep"), P()),
        out_specs=P("shard", None, "rep"),
        check_vma=False,
    )
```
